128 devices in a mesh: wall: 4 (over z), span: 32 (over y, x, core).
Axes of the slice: x: 4, y: 4, z: 4, core: 2. Of those that a mesh axis runs over, the one named last changes fastest.
Arguments:
- solution: float32 [5, 125, 32768], P(None, None, ('wall', 'span')), may hold values from -6 to 6
- level_map: int32 [32768], P(('wall', 'span')), may hold values from 0 to 3, as said below
- send_list: int32 [128, 1024], P(('wall', 'span')), may hold values from 0 to 1535, as said below
- face_partner: int32 [6, 32768], P(None, ('wall', 'span')), may hold values from 0 to 2559, as said below
- volume_block: float32 [125, 125], replicated
- lift_block: float32 [125, 150], replicated, may hold values from -0.5 to 0.5
- flux_mixing: float32 [5, 5], replicated
- metric_scale: float32 [32768], P(('wall', 'span')), may hold values from 0.5 to 2
Outputs:
- advanced_solution: float32 [5, 125, 32768], P(None, None, ('wall', 'span'))
The draws below stay inside these ranges and needn't reach their ends.
Inputs may be any that keep to these rules, and one draw needn't show every extreme that they name: `level_map`: each partition holds elements of every level. `send_list`: slot k (of 8) from any sender to any receiver names a face of a sender's element of level max(3 - j, 0), where j is the largest whole number with 2**j * (8 - k) <= 8. `face_partner`: in each partition's 256 elements, every column of the received traces is named by exactly one face; the other faces name columns of the partition's own trace table.
All inputs are finite; a program needn't handle non-finite values.
Results may differ from the reference program's by a relative error of at most 0.0001.
Values sent between devices are 32-bit elements; how exact they have to be, the bound alone decides.
No kernel may reach another device: no remote copies, remote signals or barrier semaphores. Data moves between devices by JAX's collectives and lax.ppermute only.
A program may use at most 64 MiB of HBM per device.

```python
import math
import jax
import jax.numpy as jnp
import numpy as np
from jax import lax

VARIABLES = 5
DEGREE = 4
NODES = 125
FACE_NODES = 25
TRACE_ROWS = 125
LEVELS = 4
COARSE_STEPS = 3
SLOT_COUNT = 8
DEV_ELEMENTS = 256
PARTITIONS = 128
WALL_PARTS = 4
SPAN_PARTS = 32
ELEMENTS = 32768


def slot_level_of(slot_index):
    power = 0
    while power < LEVELS - 1 and 2 ** (power + 1) * (SLOT_COUNT - slot_index) <= SLOT_COUNT:
        power = power + 1
    return max(LEVELS - 1 - power, 0)


def common_levels(key):
    level_key = jax.random.fold_in(key, 101)
    raw_level = jax.random.randint(jax.random.fold_in(level_key, 1), (ELEMENTS,), 0, 8)
    device = jnp.arange(ELEMENTS) // DEV_ELEMENTS
    wall_row = device // SPAN_PARTS
    offset = 6 * (WALL_PARTS - 1 - wall_row) // max(WALL_PARTS - 1, 1)
    levels = jnp.minimum((raw_level + offset) // 3, LEVELS - 1).astype(jnp.int32)
    levels = levels.reshape(PARTITIONS, DEV_ELEMENTS)

    def force_all(position, row):
        spots = jax.random.permutation(jax.random.fold_in(jax.random.fold_in(level_key, 2), position), DEV_ELEMENTS)[:LEVELS]
        return row.at[spots].set(jnp.arange(LEVELS, dtype=jnp.int32))
    levels = jax.vmap(force_all)(jnp.arange(PARTITIONS), levels)
    return levels.reshape(ELEMENTS).astype(jnp.int32)


def draw_level_map(key, part):
    return common_levels(key)


def draw_send_list(key, part):
    levels = common_levels(key).reshape(PARTITIONS, DEV_ELEMENTS)
    slot_table = jnp.asarray(np.array([slot_level_of(k) for k in range(SLOT_COUNT)] * PARTITIONS, dtype=np.int32))
    send_key = jax.random.fold_in(key, 202)

    def one_sender(position):
        row = levels[position]
        marks = (row[None, :] == jnp.arange(LEVELS, dtype=jnp.int32)[:, None]).astype(jnp.int32)
        running = jnp.cumsum(marks, axis=1)
        counts = running[:, -1]
        subkey = jax.random.fold_in(send_key, position)
        picks = jax.random.randint(jax.random.fold_in(subkey, 1), (PARTITIONS * SLOT_COUNT,), 0, 1 << 20)
        picks = picks % counts[slot_table]
        chosen_running = running[slot_table]
        element = jnp.sum((chosen_running < (picks + 1)[:, None]).astype(jnp.int32), axis=1)
        face = jax.random.randint(jax.random.fold_in(subkey, 2), (PARTITIONS * SLOT_COUNT,), 0, 6)
        return (face * DEV_ELEMENTS + element).astype(jnp.int32)
    return lax.map(one_sender, jnp.arange(PARTITIONS)).astype(jnp.int32)


def draw_face_partner(key, part):
    local_faces = 6 * DEV_ELEMENTS
    remote = PARTITIONS * SLOT_COUNT

    def one_partition(position):
        subkey = jax.random.fold_in(key, position)
        shuffle = jax.random.permutation(jax.random.fold_in(subkey, 1), local_faces)
        local_refs = jax.random.randint(jax.random.fold_in(subkey, 2), (local_faces,), 0, local_faces)
        ranks = jnp.arange(local_faces)
        values = jnp.where(ranks < remote, local_faces + ranks, local_refs).astype(jnp.int32)
        return jnp.zeros((local_faces,), jnp.int32).at[shuffle].set(values)
    pointer_grid = jax.vmap(one_partition)(jnp.arange(PARTITIONS))
    return pointer_grid.reshape(PARTITIONS, 6, DEV_ELEMENTS).transpose(1, 0, 2).reshape(6, ELEMENTS).astype(jnp.int32)


def dominant_block(key, order, weight):
    noise = jax.random.normal(key, (order, order), jnp.float32)
    return jnp.eye(order, dtype=jnp.float32) + weight * noise / math.sqrt(order)


def draw_volume_block(key, part):
    return dominant_block(jax.random.fold_in(key, 11), NODES, 0.3)


def draw_flux_mixing(key, part):
    return dominant_block(jax.random.fold_in(key, 17), VARIABLES, 0.4)


def shard_levels(stream_key, shape, cuts, least, high):
    def one(dim, shards_of):
        steps = jax.random.uniform(jax.random.fold_in(jax.random.fold_in(stream_key, 6), dim), (shards_of,), jnp.float32, least / len(cuts), high / len(cuts))
        return jnp.repeat(jnp.exp(steps), shape[dim] // shards_of).reshape((-1,) + (1,) * (len(shape) - dim - 1))

    gain = one(*cuts[0])
    for cut in cuts[1:]:
        gain = gain * one(*cut)
    return gain


def gaussian(stream_key, extent, deviation, limit, cuts=(), held_as=jnp.bfloat16):
    factor_of = shard_levels(stream_key, extent, cuts, -0.22, 0.18) if cuts else 1.0
    result = jax.random.normal(stream_key, extent, jnp.float32) * deviation * factor_of
    return jnp.minimum(jnp.maximum(result, -limit), limit).astype(held_as)


def setup_inputs(seed: int = 0) -> dict:
    key_of = jax.random.split(jax.random.key(seed), 9)
    return {
        "solution": gaussian(key_of[0], (VARIABLES, NODES, ELEMENTS), 1.0, 6.0, ((2, 128),), jnp.float32),
        "level_map": draw_level_map(jax.random.fold_in(key_of[8], 71), 0),
        "send_list": draw_send_list(jax.random.fold_in(key_of[8], 71), 0),
        "face_partner": draw_face_partner(jax.random.fold_in(key_of[8], 71), 0),
        "volume_block": draw_volume_block(jax.random.fold_in(key_of[8], 71), 0),
        "lift_block": gaussian(key_of[5], (NODES, 6 * FACE_NODES), (6 * FACE_NODES) ** -0.5, 0.5, (), jnp.float32),
        "flux_mixing": draw_flux_mixing(jax.random.fold_in(key_of[8], 71), 0),
        "metric_scale": jnp.clip(jnp.exp(math.log(2.0) - 1.3862944 * jax.random.uniform(key_of[7], (ELEMENTS,), jnp.float32) ** shard_levels(key_of[7], (ELEMENTS,), ((0, 128),), -0.2, 0.2)), 0.5, 2.0),
    }


COURANT = 0.6

def face_traces(fields):
    local_count = fields.shape[2]
    node_cube = fields.reshape(VARIABLES, DEGREE + 1, DEGREE + 1, DEGREE + 1, local_count)
    face_list = [node_cube[:, 0], node_cube[:, -1], node_cube[:, :, 0], node_cube[:, :, -1], node_cube[:, :, :, 0], node_cube[:, :, :, -1]]
    return jnp.stack([face.reshape(VARIABLES, FACE_NODES, local_count) for face in face_list], axis=1)

def tendency(fields, nearby, volume_block, lift_block, flux_mixing, metric_scale):
    local_count = fields.shape[2]
    own_trace = face_traces(fields).reshape(VARIABLES, 6 * FACE_NODES, local_count)
    face_jumps = nearby - own_trace
    combined = jnp.einsum('pj,vje->vpe', lift_block, face_jumps, precision=lax.Precision.HIGHEST)
    combined = combined - jnp.einsum('pq,vqe->vpe', volume_block, fields, precision=lax.Precision.HIGHEST)
    return metric_scale * jnp.einsum('vw,wpe->vpe', flux_mixing, combined, precision=lax.Precision.HIGHEST)

def take_columns(matrix, columns):
    return jnp.take(matrix, columns, axis=1)

def neighbours(fields, send_list, face_partner):
    traces = face_traces(fields)
    trace_table = traces.reshape(VARIABLES, 6, FACE_NODES, PARTITIONS, DEV_ELEMENTS).transpose(3, 0, 2, 1, 4)
    trace_table = trace_table.reshape(PARTITIONS, TRACE_ROWS, 6 * DEV_ELEMENTS)
    outgoing = jax.vmap(take_columns)(trace_table, send_list)
    received = outgoing.reshape(PARTITIONS, TRACE_ROWS, PARTITIONS, SLOT_COUNT).transpose(2, 1, 0, 3)
    received = received.reshape(PARTITIONS, TRACE_ROWS, PARTITIONS * SLOT_COUNT)
    lookup = jnp.concatenate([trace_table, received], axis=2)
    pointers = face_partner.reshape(6, PARTITIONS, DEV_ELEMENTS).transpose(1, 0, 2).reshape(PARTITIONS, 6 * DEV_ELEMENTS)
    gathered = jax.vmap(take_columns)(lookup, pointers)
    gathered = gathered.reshape(PARTITIONS, VARIABLES, FACE_NODES, 6, DEV_ELEMENTS).transpose(1, 3, 2, 0, 4)
    return gathered.reshape(VARIABLES, 6 * FACE_NODES, PARTITIONS * DEV_ELEMENTS)

def lowest_level(substep):
    for candidate in range(LEVELS):
        if substep % 2 ** (LEVELS - 1 - candidate) == 0:
            return candidate
    return LEVELS - 1

def reference(solution, level_map, send_list, face_partner, volume_block, lift_block, flux_mixing, metric_scale):
    fields = solution
    divisors = jnp.power(2, level_map).astype(jnp.float32)
    for coarse in range(COARSE_STEPS):
        element_rates = metric_scale * (1.0 + jnp.sqrt(lax.optimization_barrier(jnp.mean(fields * fields, axis=(0, 1)))))
        coarse_dt = COURANT / jnp.max(element_rates)
        step_sizes = coarse_dt / divisors
        for substep in range(2 ** (LEVELS - 1)):
            lowest = lowest_level(substep)
            nearby = neighbours(fields, send_list, face_partner)
            change = tendency(fields, nearby, volume_block, lift_block, flux_mixing, metric_scale)
            fields = fields + jnp.where(level_map >= lowest, step_sizes * change, 0.0)
    return fields
```

```python
import jax
import jax.numpy as jnp
from jax import lax
from jax.sharding import PartitionSpec as P

VARIABLES = 5
DEGREE = 4
FACE_NODES = 25
TRACE_ROWS = 125
LEVELS = 4
COARSE_STEPS = 3


COURANT = 0.6


def face_traces(fields):
    local_count = fields.shape[2]
    node_cube = fields.reshape(VARIABLES, DEGREE + 1, DEGREE + 1, DEGREE + 1, local_count)
    face_list = [
        node_cube[:, 0],
        node_cube[:, -1],
        node_cube[:, :, 0],
        node_cube[:, :, -1],
        node_cube[:, :, :, 0],
        node_cube[:, :, :, -1],
    ]
    return jnp.stack(
        [face.reshape(VARIABLES, FACE_NODES, local_count) for face in face_list], axis=1
    )


def tendency(fields, nearby, volume_block, lift_block, flux_mixing, metric_scale):
    own_trace = face_traces(fields).reshape(VARIABLES, 6 * FACE_NODES, fields.shape[2])
    face_jumps = nearby - own_trace
    combined = jnp.einsum("pj,vje->vpe", lift_block, face_jumps, precision=lax.Precision.HIGHEST)
    combined = combined - jnp.einsum(
        "pq,vqe->vpe", volume_block, fields, precision=lax.Precision.HIGHEST
    )
    return metric_scale * jnp.einsum(
        "vw,wpe->vpe", flux_mixing, combined, precision=lax.Precision.HIGHEST
    )


def arrange(columns, local_count):
    shaped = columns.reshape(VARIABLES, FACE_NODES, 6, local_count).transpose(0, 2, 1, 3)
    return shaped.reshape(VARIABLES, 6 * FACE_NODES, local_count)


def make_table(fields):
    return face_traces(fields).transpose(0, 2, 1, 3).reshape(TRACE_ROWS, 6 * fields.shape[2])


def send_slots(outgoing):
    return lax.all_to_all(outgoing, ("wall", "span"), split_axis=1, concat_axis=1, tiled=True)


def lowest_level(substep):
    for candidate in range(LEVELS):
        if substep % 2 ** (LEVELS - 1 - candidate) == 0:
            return candidate
    return LEVELS - 1


def body(
    solution,
    level_map,
    send_list,
    face_partner,
    volume_block,
    lift_block,
    flux_mixing,
    metric_scale,
):
    local_count = solution.shape[2]
    peers = lax.axis_size(("wall", "span"))
    slot_count = send_list.shape[1] // peers
    send_row = send_list[0]
    pointers = face_partner.reshape(-1)
    divisors = jnp.power(2, level_map).astype(jnp.float32)
    substeps = 2 ** (LEVELS - 1)
    start_cache = jnp.zeros((TRACE_ROWS, peers, slot_count), jnp.float32)

    def coarse_step(coarse_index, carry):
        fields, cache = carry
        element_rates = metric_scale * (1.0 + jnp.sqrt(jnp.mean(fields * fields, axis=(0, 1))))
        local_fastest = jnp.max(element_rates)
        step_sizes = None
        for substep in range(substeps):
            lowest = lowest_level(substep)
            trace_table = make_table(fields)
            outgoing = jnp.take(trace_table, send_row, axis=1)
            if substep == 0:
                rate_row = jnp.full((1, outgoing.shape[1]), local_fastest, jnp.float32)
                outgoing = jnp.concatenate([outgoing, rate_row], axis=0)
            outgoing = outgoing.reshape(outgoing.shape[0], peers, slot_count)
            received = send_slots(outgoing).reshape(outgoing.shape[0], peers * slot_count)
            if substep == 0:
                fastest = jnp.max(received[TRACE_ROWS])
                received = received[:TRACE_ROWS]
                step_sizes = COURANT / fastest / divisors
            lookup = jnp.concatenate([trace_table, received], axis=1)
            nearby = arrange(jnp.take(lookup, pointers, axis=1), local_count)
            change = tendency(fields, nearby, volume_block, lift_block, flux_mixing, metric_scale)
            fields = fields + jnp.where(level_map >= lowest, step_sizes * change, 0.0)
        return (fields, cache)

    final_fields, final_cache = lax.fori_loop(0, COARSE_STEPS, coarse_step, (solution, start_cache))
    return final_fields


def solution(mesh):
    return jax.shard_map(
        body,
        mesh=mesh,
        in_specs=(
            P(None, None, ("wall", "span")),
            P(("wall", "span")),
            P(("wall", "span"), None),
            P(None, ("wall", "span")),
            P(),
            P(),
            P(),
            P(("wall", "span")),
        ),
        out_specs=P(None, None, ("wall", "span")),
        check_vma=False,
    )
```

```python
import numpy as np
import jax
import jax.numpy as jnp
from jax import lax
from jax.sharding import PartitionSpec as P

VARIABLES = 5
DEGREE = 4
NODES = 125
FACE_NODES = 25
TRACE_ROWS = 125
LEVELS = 4
COARSE_STEPS = 3
FACES = 6


COURANT = 0.6
HIGHEST = lax.Precision.HIGHEST


def face_node_table():
    cube = np.arange(NODES).reshape(DEGREE + 1, DEGREE + 1, DEGREE + 1)
    faces = [cube[0], cube[-1], cube[:, 0], cube[:, -1], cube[:, :, 0], cube[:, :, -1]]
    return np.stack([face.reshape(FACE_NODES) for face in faces]).astype(np.int32)


def selection_matrix():
    nodes = jnp.asarray(face_node_table())
    row_v = lax.broadcasted_iota(jnp.int32, (VARIABLES * NODES, FACES, VARIABLES, FACE_NODES), 0) // NODES
    row_n = lax.broadcasted_iota(jnp.int32, (VARIABLES * NODES, FACES, VARIABLES, FACE_NODES), 0) % NODES
    col_v = lax.broadcasted_iota(jnp.int32, (VARIABLES * NODES, FACES, VARIABLES, FACE_NODES), 2)
    hit = (row_v == col_v) & (row_n == nodes[None, :, None, :])
    return hit.astype(jnp.float32).reshape(VARIABLES * NODES, FACES * TRACE_ROWS)


def lowest_level(substep):
    for candidate in range(LEVELS):
        if substep % 2 ** (LEVELS - 1 - candidate) == 0:
            return candidate
    return LEVELS - 1


def body(
    solution,
    level_map,
    send_list,
    face_partner,
    volume_block,
    lift_block,
    flux_mixing,
    metric_scale,
):
    local_count = solution.shape[2]
    peers = lax.axis_size(("wall", "span"))
    slot_count = send_list.shape[1] // peers
    own_faces = FACES * local_count

    def table_row(column):
        return (column % local_count) * FACES + column // local_count

    send_rows = table_row(send_list[0])
    partner = face_partner.T.reshape(-1)
    partner_rows = jnp.where(partner < own_faces, table_row(partner), partner)

    select = selection_matrix()
    lift3 = lift_block.reshape(NODES, FACES, FACE_NODES)
    lift_op = (
        flux_mixing.T[None, :, None, :, None] * lift3.transpose(1, 2, 0)[:, None, :, None, :]
    ).reshape(FACES * TRACE_ROWS, VARIABLES * NODES)
    volume_op = (flux_mixing.T[:, None, :, None] * volume_block.T[None, :, None, :]).reshape(
        VARIABLES * NODES, VARIABLES * NODES
    )

    fields = solution.transpose(2, 0, 1).reshape(local_count, VARIABLES * NODES)
    metric = metric_scale[:, None]
    divisors = jnp.power(2, level_map).astype(jnp.float32)
    substeps = 2 ** (LEVELS - 1)

    def coarse_step(coarse_index, fields):
        element_rates = metric_scale * (1.0 + jnp.sqrt(jnp.mean(fields * fields, axis=1)))
        local_fastest = jnp.max(element_rates)
        step_sizes = None
        for substep in range(substeps):
            lowest = lowest_level(substep)
            traces = jnp.dot(fields, select, precision=HIGHEST)
            table = traces.reshape(own_faces, TRACE_ROWS)
            outgoing = jnp.take(table, send_rows, axis=0)
            if substep == 0:
                rate_column = jnp.full((outgoing.shape[0], 1), local_fastest, jnp.float32)
                outgoing = jnp.concatenate([outgoing, rate_column], axis=1)
            outgoing = outgoing.reshape(peers, slot_count, outgoing.shape[1])
            received = lax.all_to_all(
                outgoing, ("wall", "span"), split_axis=0, concat_axis=0, tiled=True
            ).reshape(peers * slot_count, outgoing.shape[2])
            if substep == 0:
                fastest = jnp.max(received[:, TRACE_ROWS])
                received = received[:, :TRACE_ROWS]
                step_sizes = (COURANT / fastest / divisors)[:, None]
            lookup = jnp.concatenate([table, received], axis=0)
            nearby = jnp.take(lookup, partner_rows, axis=0).reshape(
                local_count, FACES * TRACE_ROWS
            )
            change = metric * (
                jnp.dot(nearby - traces, lift_op, precision=HIGHEST)
                - jnp.dot(fields, volume_op, precision=HIGHEST)
            )
            active = (level_map >= lowest)[:, None]
            fields = fields + jnp.where(active, step_sizes * change, 0.0)
        return fields

    final_fields = lax.fori_loop(0, COARSE_STEPS, coarse_step, fields)
    return final_fields.reshape(local_count, VARIABLES, NODES).transpose(1, 2, 0)


def solution(mesh):
    return jax.shard_map(
        body,
        mesh=mesh,
        in_specs=(
            P(None, None, ("wall", "span")),
            P(("wall", "span")),
            P(("wall", "span"), None),
            P(None, ("wall", "span")),
            P(),
            P(),
            P(),
            P(("wall", "span")),
        ),
        out_specs=P(None, None, ("wall", "span")),
        check_vma=False,
    )
```

```python
import jax
import jax.numpy as jnp
from jax import lax
from jax.sharding import PartitionSpec as P

VARIABLES = 5
DEGREE = 4
FACE_NODES = 25
TRACE_ROWS = 125
LEVELS = 4
COARSE_STEPS = 3


COURANT = 0.6


def face_traces(fields):
    local_count = fields.shape[2]
    node_cube = fields.reshape(VARIABLES, DEGREE + 1, DEGREE + 1, DEGREE + 1, local_count)
    face_list = [
        node_cube[:, 0],
        node_cube[:, -1],
        node_cube[:, :, 0],
        node_cube[:, :, -1],
        node_cube[:, :, :, 0],
        node_cube[:, :, :, -1],
    ]
    return jnp.stack(
        [face.reshape(VARIABLES, FACE_NODES, local_count) for face in face_list], axis=1
    )


def tendency(fields, nearby, volume_block, lift_block, flux_mixing, metric_scale):
    own_trace = face_traces(fields).reshape(VARIABLES, 6 * FACE_NODES, fields.shape[2])
    face_jumps = nearby - own_trace
    combined = jnp.einsum("pj,vje->vpe", lift_block, face_jumps, precision=lax.Precision.HIGHEST)
    combined = combined - jnp.einsum(
        "pq,vqe->vpe", volume_block, fields, precision=lax.Precision.HIGHEST
    )
    return metric_scale * jnp.einsum(
        "vw,wpe->vpe", flux_mixing, combined, precision=lax.Precision.HIGHEST
    )


def arrange(columns, local_count):
    shaped = columns.reshape(VARIABLES, FACE_NODES, 6, local_count).transpose(0, 2, 1, 3)
    return shaped.reshape(VARIABLES, 6 * FACE_NODES, local_count)


def make_table(fields):
    return face_traces(fields).transpose(0, 2, 1, 3).reshape(TRACE_ROWS, 6 * fields.shape[2])


def send_slots(outgoing):
    return lax.all_to_all(outgoing, ("wall", "span"), split_axis=1, concat_axis=1, tiled=True)


def lowest_level(substep):
    for candidate in range(LEVELS):
        if substep % 2 ** (LEVELS - 1 - candidate) == 0:
            return candidate
    return LEVELS - 1


def body(
    solution,
    level_map,
    send_list,
    face_partner,
    volume_block,
    lift_block,
    flux_mixing,
    metric_scale,
):
    local_count = solution.shape[2]
    peers = lax.axis_size(("wall", "span"))
    slot_count = send_list.shape[1] // peers
    send_row = send_list[0]
    pointers = face_partner.reshape(-1)
    own_columns = 6 * local_count
    local_pointers = jnp.where(pointers < own_columns, pointers, own_columns)
    remote_pointers = jnp.where(
        pointers >= own_columns, pointers - own_columns, peers * slot_count
    )
    divisors = jnp.power(2, level_map).astype(jnp.float32)
    substeps = 2 ** (LEVELS - 1)
    start_cache = jnp.zeros((TRACE_ROWS, peers, slot_count), jnp.float32)

    def coarse_step(coarse_index, carry):
        fields, cache = carry
        element_rates = metric_scale * (1.0 + jnp.sqrt(jnp.mean(fields * fields, axis=(0, 1))))
        local_fastest = jnp.max(element_rates)
        step_sizes = None
        for substep in range(substeps):
            lowest = lowest_level(substep)
            trace_table = make_table(fields)
            outgoing = jnp.take(trace_table, send_row, axis=1)
            if substep == 0:
                rate_row = jnp.full((1, outgoing.shape[1]), local_fastest, jnp.float32)
                outgoing = jnp.concatenate([outgoing, rate_row], axis=0)
            outgoing = outgoing.reshape(outgoing.shape[0], peers, slot_count)
            received = send_slots(outgoing).reshape(outgoing.shape[0], peers * slot_count)
            if substep == 0:
                fastest = jnp.max(received[TRACE_ROWS])
                received = received[:TRACE_ROWS]
                step_sizes = COURANT / fastest / divisors
            lift4 = lift_block.reshape(TRACE_ROWS, 6, FACE_NODES)
            own_table = trace_table.reshape(VARIABLES, FACE_NODES, 6, local_count)
            local_lookup = jnp.concatenate(
                [trace_table, jnp.zeros((TRACE_ROWS, 1), jnp.float32)], axis=1
            )
            local_near = jnp.take(local_lookup, local_pointers, axis=1).reshape(
                VARIABLES, FACE_NODES, 6, local_count
            )
            before = jnp.einsum(
                "pfn,vnfe->vpe", lift4, local_near - own_table, precision=lax.Precision.HIGHEST
            ) - jnp.einsum("pq,vqe->vpe", volume_block, fields, precision=lax.Precision.HIGHEST)
            remote_lookup = jnp.concatenate(
                [received, jnp.zeros((TRACE_ROWS, 1), jnp.float32)], axis=1
            )
            remote_near = jnp.take(remote_lookup, remote_pointers, axis=1).reshape(
                VARIABLES, FACE_NODES, 6, local_count
            )
            combined = before + jnp.einsum(
                "pfn,vnfe->vpe", lift4, remote_near, precision=lax.Precision.HIGHEST
            )
            change = metric_scale * jnp.einsum(
                "vw,wpe->vpe", flux_mixing, combined, precision=lax.Precision.HIGHEST
            )
            fields = fields + jnp.where(level_map >= lowest, step_sizes * change, 0.0)
        return (fields, cache)

    final_fields, final_cache = lax.fori_loop(0, COARSE_STEPS, coarse_step, (solution, start_cache))
    return final_fields


def solution(mesh):
    return jax.shard_map(
        body,
        mesh=mesh,
        in_specs=(
            P(None, None, ("wall", "span")),
            P(("wall", "span")),
            P(("wall", "span"), None),
            P(None, ("wall", "span")),
            P(),
            P(),
            P(),
            P(("wall", "span")),
        ),
        out_specs=P(None, None, ("wall", "span")),
        check_vma=False,
    )
```

```python
import jax
import jax.numpy as jnp
from jax import lax
from jax.sharding import PartitionSpec as P

VARIABLES = 5
DEGREE = 4
FACE_NODES = 25
TRACE_ROWS = 125
LEVELS = 4
COARSE_STEPS = 3


COURANT = 0.6


def face_traces(fields):
    local_count = fields.shape[2]
    node_cube = fields.reshape(VARIABLES, DEGREE + 1, DEGREE + 1, DEGREE + 1, local_count)
    face_list = [
        node_cube[:, 0],
        node_cube[:, -1],
        node_cube[:, :, 0],
        node_cube[:, :, -1],
        node_cube[:, :, :, 0],
        node_cube[:, :, :, -1],
    ]
    return jnp.stack(
        [face.reshape(VARIABLES, FACE_NODES, local_count) for face in face_list], axis=1
    )


def tendency(fields, nearby, volume_block, lift_block, flux_mixing, metric_scale):
    own_trace = face_traces(fields).reshape(VARIABLES, 6 * FACE_NODES, fields.shape[2])
    face_jumps = nearby - own_trace
    combined = jnp.einsum("pj,vje->vpe", lift_block, face_jumps, precision=lax.Precision.HIGHEST)
    combined = combined - jnp.einsum(
        "pq,vqe->vpe", volume_block, fields, precision=lax.Precision.HIGHEST
    )
    return metric_scale * jnp.einsum(
        "vw,wpe->vpe", flux_mixing, combined, precision=lax.Precision.HIGHEST
    )


def arrange(columns, local_count):
    shaped = columns.reshape(VARIABLES, FACE_NODES, 6, local_count).transpose(0, 2, 1, 3)
    return shaped.reshape(VARIABLES, 6 * FACE_NODES, local_count)


def make_table(fields):
    return face_traces(fields).transpose(0, 2, 1, 3).reshape(TRACE_ROWS, 6 * fields.shape[2])


def send_slots(outgoing):
    return lax.all_to_all(outgoing, ("wall", "span"), split_axis=1, concat_axis=1, tiled=True)


def lowest_level(substep):
    for candidate in range(LEVELS):
        if substep % 2 ** (LEVELS - 1 - candidate) == 0:
            return candidate
    return LEVELS - 1


def slot_level(slot, slot_count):
    power = 0
    while power < LEVELS - 1 and 2 ** (power + 1) * (slot_count - slot) <= slot_count:
        power = power + 1
    return max(LEVELS - 1 - power, 0)


def changed_slots(substep, slot_count):
    if substep == 0:
        return slot_count
    previous = lowest_level(substep - 1)
    levels = [slot_level(k, slot_count) for k in range(slot_count)]
    assert levels == sorted(levels, reverse=True)
    return sum(1 for level in levels if level >= previous)


def body(
    solution,
    level_map,
    send_list,
    face_partner,
    volume_block,
    lift_block,
    flux_mixing,
    metric_scale,
):
    local_count = solution.shape[2]
    peers = lax.axis_size(("wall", "span"))
    slot_count = send_list.shape[1] // peers
    send_row = send_list[0]
    pointers = face_partner.reshape(-1)
    divisors = jnp.power(2, level_map).astype(jnp.float32)
    substeps = 2 ** (LEVELS - 1)
    start_cache = jnp.zeros((TRACE_ROWS, peers, slot_count), jnp.float32)

    def coarse_step(coarse_index, carry):
        fields, cache = carry
        element_rates = metric_scale * (1.0 + jnp.sqrt(jnp.mean(fields * fields, axis=(0, 1))))
        local_fastest = jnp.max(element_rates)
        step_sizes = None
        received = None
        for substep in range(substeps):
            lowest = lowest_level(substep)
            fresh = changed_slots(substep, slot_count)
            trace_table = make_table(fields)
            send_columns = send_row.reshape(peers, slot_count)[:, :fresh].reshape(-1)
            outgoing = jnp.take(trace_table, send_columns, axis=1)
            if substep == 0:
                rate_row = jnp.full((1, outgoing.shape[1]), local_fastest, jnp.float32)
                outgoing = jnp.concatenate([outgoing, rate_row], axis=0)
            outgoing = outgoing.reshape(outgoing.shape[0], peers, fresh)
            arrived = send_slots(outgoing)
            if substep == 0:
                fastest = jnp.max(arrived[TRACE_ROWS])
                arrived = arrived[:TRACE_ROWS]
                step_sizes = COURANT / fastest / divisors
            if fresh < slot_count:
                arrived = jnp.concatenate([arrived, received[:, :, fresh:]], axis=2)
            received = arrived
            received_flat = received.reshape(TRACE_ROWS, peers * slot_count)
            lookup = jnp.concatenate([trace_table, received_flat], axis=1)
            nearby = arrange(jnp.take(lookup, pointers, axis=1), local_count)
            change = tendency(fields, nearby, volume_block, lift_block, flux_mixing, metric_scale)
            fields = fields + jnp.where(level_map >= lowest, step_sizes * change, 0.0)
        return (fields, cache)

    final_fields, final_cache = lax.fori_loop(0, COARSE_STEPS, coarse_step, (solution, start_cache))
    return final_fields


def solution(mesh):
    return jax.shard_map(
        body,
        mesh=mesh,
        in_specs=(
            P(None, None, ("wall", "span")),
            P(("wall", "span")),
            P(("wall", "span"), None),
            P(None, ("wall", "span")),
            P(),
            P(),
            P(),
            P(("wall", "span")),
        ),
        out_specs=P(None, None, ("wall", "span")),
        check_vma=False,
    )
```

```python
import jax
import jax.numpy as jnp
from jax import lax
from jax.sharding import PartitionSpec as P

VARIABLES = 5
DEGREE = 4
FACE_NODES = 25
TRACE_ROWS = 125
LEVELS = 4
COARSE_STEPS = 3


COURANT = 0.6


def face_traces(fields):
    local_count = fields.shape[2]
    node_cube = fields.reshape(VARIABLES, DEGREE + 1, DEGREE + 1, DEGREE + 1, local_count)
    face_list = [
        node_cube[:, 0],
        node_cube[:, -1],
        node_cube[:, :, 0],
        node_cube[:, :, -1],
        node_cube[:, :, :, 0],
        node_cube[:, :, :, -1],
    ]
    return jnp.stack(
        [face.reshape(VARIABLES, FACE_NODES, local_count) for face in face_list], axis=1
    )


def tendency(fields, nearby, volume_block, lift_block, flux_mixing, metric_scale):
    own_trace = face_traces(fields).reshape(VARIABLES, 6 * FACE_NODES, fields.shape[2])
    face_jumps = nearby - own_trace
    combined = jnp.einsum("pj,vje->vpe", lift_block, face_jumps, precision=lax.Precision.HIGH)
    combined = combined - jnp.einsum(
        "pq,vqe->vpe", volume_block, fields, precision=lax.Precision.HIGH
    )
    return metric_scale * jnp.einsum(
        "vw,wpe->vpe", flux_mixing, combined, precision=lax.Precision.HIGH
    )


def arrange(columns, local_count):
    shaped = columns.reshape(VARIABLES, FACE_NODES, 6, local_count).transpose(0, 2, 1, 3)
    return shaped.reshape(VARIABLES, 6 * FACE_NODES, local_count)


def make_table(fields):
    return face_traces(fields).transpose(0, 2, 1, 3).reshape(TRACE_ROWS, 6 * fields.shape[2])


def send_slots(outgoing):
    return lax.all_to_all(outgoing, ("wall", "span"), split_axis=1, concat_axis=1, tiled=True)


def lowest_level(substep):
    for candidate in range(LEVELS):
        if substep % 2 ** (LEVELS - 1 - candidate) == 0:
            return candidate
    return LEVELS - 1


def slot_level(slot, slot_count):
    power = 0
    while power < LEVELS - 1 and 2 ** (power + 1) * (slot_count - slot) <= slot_count:
        power = power + 1
    return max(LEVELS - 1 - power, 0)


def changed_slots(substep, slot_count):
    if substep == 0:
        return slot_count
    previous = lowest_level(substep - 1)
    levels = [slot_level(k, slot_count) for k in range(slot_count)]
    assert levels == sorted(levels, reverse=True)
    return sum(1 for level in levels if level >= previous)


def body(
    solution,
    level_map,
    send_list,
    face_partner,
    volume_block,
    lift_block,
    flux_mixing,
    metric_scale,
):
    local_count = solution.shape[2]
    peers = lax.axis_size(("wall", "span"))
    slot_count = send_list.shape[1] // peers
    send_row = send_list[0]
    pointers = face_partner.reshape(-1)
    divisors = jnp.power(2, level_map).astype(jnp.float32)
    substeps = 2 ** (LEVELS - 1)
    start_cache = jnp.zeros((TRACE_ROWS, peers, slot_count), jnp.float32)

    def coarse_step(coarse_index, carry):
        fields, cache = carry
        element_rates = metric_scale * (1.0 + jnp.sqrt(jnp.mean(fields * fields, axis=(0, 1))))
        local_fastest = jnp.max(element_rates)
        step_sizes = None
        received = None
        for substep in range(substeps):
            lowest = lowest_level(substep)
            fresh = changed_slots(substep, slot_count)
            trace_table = make_table(fields)
            send_columns = send_row.reshape(peers, slot_count)[:, :fresh].reshape(-1)
            outgoing = jnp.take(trace_table, send_columns, axis=1)
            if substep == 0:
                rate_row = jnp.full((1, outgoing.shape[1]), local_fastest, jnp.float32)
                outgoing = jnp.concatenate([outgoing, rate_row], axis=0)
            outgoing = outgoing.reshape(outgoing.shape[0], peers, fresh)
            arrived = send_slots(outgoing)
            if substep == 0:
                fastest = jnp.max(arrived[TRACE_ROWS])
                arrived = arrived[:TRACE_ROWS]
                step_sizes = COURANT / fastest / divisors
            if fresh < slot_count:
                arrived = jnp.concatenate([arrived, received[:, :, fresh:]], axis=2)
            received = arrived
            received_flat = received.reshape(TRACE_ROWS, peers * slot_count)
            lookup = jnp.concatenate([trace_table, received_flat], axis=1)
            nearby = arrange(jnp.take(lookup, pointers, axis=1), local_count)
            change = tendency(fields, nearby, volume_block, lift_block, flux_mixing, metric_scale)
            fields = fields + jnp.where(level_map >= lowest, step_sizes * change, 0.0)
        return (fields, cache)

    final_fields, final_cache = lax.fori_loop(0, COARSE_STEPS, coarse_step, (solution, start_cache))
    return final_fields


def solution(mesh):
    return jax.shard_map(
        body,
        mesh=mesh,
        in_specs=(
            P(None, None, ("wall", "span")),
            P(("wall", "span")),
            P(("wall", "span"), None),
            P(None, ("wall", "span")),
            P(),
            P(),
            P(),
            P(("wall", "span")),
        ),
        out_specs=P(None, None, ("wall", "span")),
        check_vma=False,
    )
```

```python
import jax
import jax.numpy as jnp
from jax import lax
from jax.sharding import PartitionSpec as P

VARIABLES = 5
DEGREE = 4
FACE_NODES = 25
TRACE_ROWS = 125
LEVELS = 4
COARSE_STEPS = 3


COURANT = 0.6


def face_traces(fields):
    local_count = fields.shape[2]
    node_cube = fields.reshape(VARIABLES, DEGREE + 1, DEGREE + 1, DEGREE + 1, local_count)
    face_list = [
        node_cube[:, 0],
        node_cube[:, -1],
        node_cube[:, :, 0],
        node_cube[:, :, -1],
        node_cube[:, :, :, 0],
        node_cube[:, :, :, -1],
    ]
    return jnp.stack(
        [face.reshape(VARIABLES, FACE_NODES, local_count) for face in face_list], axis=1
    )


def tendency(fields, nearby, volume_block, lift_block, flux_mixing, metric_scale):
    own_trace = face_traces(fields).reshape(VARIABLES, 6 * FACE_NODES, fields.shape[2])
    face_jumps = nearby - own_trace
    combined = jnp.einsum("pj,vje->vpe", lift_block, face_jumps, precision=lax.Precision.HIGH)
    combined = combined - jnp.einsum(
        "pq,vqe->vpe", volume_block, fields, precision=lax.Precision.HIGH
    )
    return metric_scale * jnp.einsum(
        "vw,wpe->vpe", flux_mixing, combined, precision=lax.Precision.HIGH
    )


def arrange(columns, local_count):
    shaped = columns.reshape(VARIABLES, FACE_NODES, 6, local_count).transpose(0, 2, 1, 3)
    return shaped.reshape(VARIABLES, 6 * FACE_NODES, local_count)


def make_table(fields):
    return face_traces(fields).transpose(0, 2, 1, 3).reshape(TRACE_ROWS, 6 * fields.shape[2])


def send_slots(outgoing):
    return lax.all_to_all(outgoing, ("wall", "span"), split_axis=1, concat_axis=1, tiled=True)


def lowest_level(substep):
    for candidate in range(LEVELS):
        if substep % 2 ** (LEVELS - 1 - candidate) == 0:
            return candidate
    return LEVELS - 1


def slot_level(slot, slot_count):
    power = 0
    while power < LEVELS - 1 and 2 ** (power + 1) * (slot_count - slot) <= slot_count:
        power = power + 1
    return max(LEVELS - 1 - power, 0)


def changed_slots(substep, slot_count):
    if substep == 0:
        return slot_count
    previous = lowest_level(substep - 1)
    levels = [slot_level(k, slot_count) for k in range(slot_count)]
    assert levels == sorted(levels, reverse=True)
    return sum(1 for level in levels if level >= previous)


def body(
    solution,
    level_map,
    send_list,
    face_partner,
    volume_block,
    lift_block,
    flux_mixing,
    metric_scale,
):
    local_count = solution.shape[2]
    peers = lax.axis_size(("wall", "span"))
    slot_count = send_list.shape[1] // peers
    send_row = send_list[0]
    pointers = face_partner.reshape(-1)
    divisors = jnp.power(2, level_map).astype(jnp.float32)
    substeps = 2 ** (LEVELS - 1)
    start_cache = jnp.zeros((TRACE_ROWS, peers, slot_count), jnp.float32)

    def coarse_step(coarse_index, carry):
        fields, cache = carry
        element_rates = metric_scale * (1.0 + jnp.sqrt(jnp.mean(fields * fields, axis=(0, 1))))
        local_fastest = jnp.max(element_rates)
        step_sizes = None
        received = None
        for substep in range(substeps):
            lowest = lowest_level(substep)
            fresh = changed_slots(substep, slot_count)
            trace_table = make_table(fields)
            send_columns = send_row.reshape(peers, slot_count)[:, :fresh].reshape(-1)
            outgoing = trace_table.at[:, send_columns].get(mode="promise_in_bounds")
            if substep == 0:
                rate_row = jnp.full((1, outgoing.shape[1]), local_fastest, jnp.float32)
                outgoing = jnp.concatenate([outgoing, rate_row], axis=0)
            outgoing = outgoing.reshape(outgoing.shape[0], peers, fresh)
            arrived = send_slots(outgoing)
            if substep == 0:
                fastest = jnp.max(arrived[TRACE_ROWS])
                arrived = arrived[:TRACE_ROWS]
                step_sizes = COURANT / fastest / divisors
            if fresh < slot_count:
                arrived = jnp.concatenate([arrived, received[:, :, fresh:]], axis=2)
            received = arrived
            received_flat = received.reshape(TRACE_ROWS, peers * slot_count)
            lookup = jnp.concatenate([trace_table, received_flat], axis=1)
            nearby = arrange(lookup.at[:, pointers].get(mode="promise_in_bounds"), local_count)
            change = tendency(fields, nearby, volume_block, lift_block, flux_mixing, metric_scale)
            fields = fields + jnp.where(level_map >= lowest, step_sizes * change, 0.0)
        return (fields, cache)

    final_fields, final_cache = lax.fori_loop(0, COARSE_STEPS, coarse_step, (solution, start_cache))
    return final_fields


def solution(mesh):
    return jax.shard_map(
        body,
        mesh=mesh,
        in_specs=(
            P(None, None, ("wall", "span")),
            P(("wall", "span")),
            P(("wall", "span"), None),
            P(None, ("wall", "span")),
            P(),
            P(),
            P(),
            P(("wall", "span")),
        ),
        out_specs=P(None, None, ("wall", "span")),
        check_vma=False,
    )
```

```python
import jax
import jax.numpy as jnp
from jax import lax
from jax.sharding import PartitionSpec as P

VARIABLES = 5
DEGREE = 4
FACE_NODES = 25
TRACE_ROWS = 125
LEVELS = 4
COARSE_STEPS = 3


COURANT = 0.6


def face_traces(fields):
    local_count = fields.shape[2]
    node_cube = fields.reshape(VARIABLES, DEGREE + 1, DEGREE + 1, DEGREE + 1, local_count)
    face_list = [
        node_cube[:, 0],
        node_cube[:, -1],
        node_cube[:, :, 0],
        node_cube[:, :, -1],
        node_cube[:, :, :, 0],
        node_cube[:, :, :, -1],
    ]
    return jnp.stack(
        [face.reshape(VARIABLES, FACE_NODES, local_count) for face in face_list], axis=1
    )


def tendency(fields, nearby, volume_block, lift_block, flux_mixing, metric_scale):
    own_trace = face_traces(fields).reshape(VARIABLES, 6 * FACE_NODES, fields.shape[2])
    face_jumps = nearby - own_trace
    combined = jnp.einsum("pj,vje->vpe", lift_block, face_jumps, precision=lax.Precision.HIGH)
    combined = combined - jnp.einsum(
        "pq,vqe->vpe", volume_block, fields, precision=lax.Precision.HIGH
    )
    return metric_scale * jnp.einsum(
        "vw,wpe->vpe", flux_mixing, combined, precision=lax.Precision.HIGH
    )


def arrange(columns, local_count):
    shaped = columns.reshape(VARIABLES, FACE_NODES, 6, local_count).transpose(0, 2, 1, 3)
    return shaped.reshape(VARIABLES, 6 * FACE_NODES, local_count)


def make_table(fields):
    return face_traces(fields).transpose(0, 2, 1, 3).reshape(TRACE_ROWS, 6 * fields.shape[2])


def send_slots(outgoing):
    return lax.all_to_all(outgoing, ("wall", "span"), split_axis=1, concat_axis=1, tiled=True)


def lowest_level(substep):
    for candidate in range(LEVELS):
        if substep % 2 ** (LEVELS - 1 - candidate) == 0:
            return candidate
    return LEVELS - 1


def slot_level(slot, slot_count):
    power = 0
    while power < LEVELS - 1 and 2 ** (power + 1) * (slot_count - slot) <= slot_count:
        power = power + 1
    return max(LEVELS - 1 - power, 0)


def changed_slots(substep, slot_count):
    if substep == 0:
        return slot_count
    previous = lowest_level(substep - 1)
    levels = [slot_level(k, slot_count) for k in range(slot_count)]
    assert levels == sorted(levels, reverse=True)
    return sum(1 for level in levels if level >= previous)


def body(
    solution,
    level_map,
    send_list,
    face_partner,
    volume_block,
    lift_block,
    flux_mixing,
    metric_scale,
):
    local_count = solution.shape[2]
    peers = lax.axis_size(("wall", "span"))
    slot_count = send_list.shape[1] // peers
    send_row = send_list[0]
    pointers = face_partner.reshape(-1)
    divisors = jnp.power(2, level_map).astype(jnp.float32)
    substeps = 2 ** (LEVELS - 1)
    start_cache = jnp.zeros((TRACE_ROWS, peers, slot_count), jnp.float32)

    def coarse_step(coarse_index, carry):
        fields, cache = carry
        element_rates = metric_scale * (1.0 + jnp.sqrt(jnp.mean(fields * fields, axis=(0, 1))))
        local_fastest = jnp.max(element_rates)
        step_sizes = None
        received = None
        for substep in range(substeps):
            lowest = lowest_level(substep)
            fresh = changed_slots(substep, slot_count)
            trace_table = make_table(fields)
            table_rows = trace_table.T
            send_columns = send_row.reshape(peers, slot_count)[:, :fresh].reshape(-1)
            outgoing = table_rows.at[send_columns].get(mode="promise_in_bounds")
            if substep == 0:
                rate_column = jnp.full((outgoing.shape[0], 1), local_fastest, jnp.float32)
                outgoing = jnp.concatenate([outgoing, rate_column], axis=1)
            outgoing = outgoing.reshape(peers, fresh, outgoing.shape[1])
            arrived = lax.all_to_all(
                outgoing, ("wall", "span"), split_axis=0, concat_axis=0, tiled=True
            )
            if substep == 0:
                fastest = jnp.max(arrived[:, :, TRACE_ROWS])
                arrived = arrived[:, :, :TRACE_ROWS]
                step_sizes = COURANT / fastest / divisors
            if fresh < slot_count:
                arrived = jnp.concatenate([arrived, received[:, fresh:]], axis=1)
            received = arrived
            lookup = jnp.concatenate(
                [table_rows, received.reshape(peers * slot_count, TRACE_ROWS)], axis=0
            )
            nearby = arrange(lookup.at[pointers].get(mode="promise_in_bounds").T, local_count)
            change = tendency(fields, nearby, volume_block, lift_block, flux_mixing, metric_scale)
            fields = fields + jnp.where(level_map >= lowest, step_sizes * change, 0.0)
        return (fields, cache)

    final_fields, final_cache = lax.fori_loop(0, COARSE_STEPS, coarse_step, (solution, start_cache))
    return final_fields


def solution(mesh):
    return jax.shard_map(
        body,
        mesh=mesh,
        in_specs=(
            P(None, None, ("wall", "span")),
            P(("wall", "span")),
            P(("wall", "span"), None),
            P(None, ("wall", "span")),
            P(),
            P(),
            P(),
            P(("wall", "span")),
        ),
        out_specs=P(None, None, ("wall", "span")),
        check_vma=False,
    )
```

```python
import jax
import jax.numpy as jnp
from jax import lax
from jax.sharding import PartitionSpec as P

VARIABLES = 5
DEGREE = 4
FACE_NODES = 25
TRACE_ROWS = 125
LEVELS = 4
COARSE_STEPS = 3


COURANT = 0.6


def face_traces(fields):
    local_count = fields.shape[2]
    node_cube = fields.reshape(VARIABLES, DEGREE + 1, DEGREE + 1, DEGREE + 1, local_count)
    face_list = [
        node_cube[:, 0],
        node_cube[:, -1],
        node_cube[:, :, 0],
        node_cube[:, :, -1],
        node_cube[:, :, :, 0],
        node_cube[:, :, :, -1],
    ]
    return jnp.stack(
        [face.reshape(VARIABLES, FACE_NODES, local_count) for face in face_list], axis=1
    )


def tendency(fields, nearby, volume_block, lift_block, flux_mixing, metric_scale):
    own_trace = face_traces(fields).reshape(VARIABLES, 6 * FACE_NODES, fields.shape[2])
    face_jumps = nearby - own_trace
    combined = jnp.einsum("pj,vje->vpe", lift_block, face_jumps, precision=lax.Precision.HIGH)
    combined = combined - jnp.einsum(
        "pq,vqe->vpe", volume_block, fields, precision=lax.Precision.HIGH
    )
    return metric_scale * jnp.einsum(
        "vw,wpe->vpe", flux_mixing, combined, precision=lax.Precision.HIGH
    )


def arrange(columns, local_count):
    shaped = columns.reshape(VARIABLES, FACE_NODES, 6, local_count).transpose(0, 2, 1, 3)
    return shaped.reshape(VARIABLES, 6 * FACE_NODES, local_count)


def make_table(fields):
    return face_traces(fields).transpose(0, 2, 1, 3).reshape(TRACE_ROWS, 6 * fields.shape[2])


def send_slots(outgoing):
    return lax.all_to_all(outgoing, ("wall", "span"), split_axis=1, concat_axis=1, tiled=True)


def lowest_level(substep):
    for candidate in range(LEVELS):
        if substep % 2 ** (LEVELS - 1 - candidate) == 0:
            return candidate
    return LEVELS - 1


def slot_level(slot, slot_count):
    power = 0
    while power < LEVELS - 1 and 2 ** (power + 1) * (slot_count - slot) <= slot_count:
        power = power + 1
    return max(LEVELS - 1 - power, 0)


def changed_slots(substep, slot_count):
    if substep == 0:
        return slot_count
    previous = lowest_level(substep - 1)
    levels = [slot_level(k, slot_count) for k in range(slot_count)]
    assert levels == sorted(levels, reverse=True)
    return sum(1 for level in levels if level >= previous)


def body(
    solution,
    level_map,
    send_list,
    face_partner,
    volume_block,
    lift_block,
    flux_mixing,
    metric_scale,
):
    local_count = solution.shape[2]
    peers = lax.axis_size(("wall", "span"))
    slot_count = send_list.shape[1] // peers
    send_row = send_list[0]
    pointers = face_partner.reshape(-1)
    divisors = jnp.power(2, level_map).astype(jnp.float32)
    lift_faces = lift_block.reshape(TRACE_ROWS, 6, FACE_NODES).transpose(1, 0, 2)
    lift_big = (
        jnp.eye(VARIABLES, dtype=jnp.float32)[None, :, None, :, None] * lift_faces[:, None, :, None, :]
    ).reshape(6, VARIABLES, TRACE_ROWS, TRACE_ROWS)
    substeps = 2 ** (LEVELS - 1)
    start_cache = jnp.zeros((TRACE_ROWS, peers, slot_count), jnp.float32)

    def coarse_step(coarse_index, carry):
        fields, cache = carry
        element_rates = metric_scale * (1.0 + jnp.sqrt(jnp.mean(fields * fields, axis=(0, 1))))
        local_fastest = jnp.max(element_rates)
        step_sizes = None
        received = None
        for substep in range(substeps):
            lowest = lowest_level(substep)
            fresh = changed_slots(substep, slot_count)
            trace_table = make_table(fields)
            table_rows = trace_table.T
            send_columns = send_row.reshape(peers, slot_count)[:, :fresh]
            outgoing = table_rows.at[send_columns].get(mode="promise_in_bounds")
            if substep == 0:
                rate_column = jnp.full((peers, fresh, 1), local_fastest, jnp.float32)
                outgoing = jnp.concatenate([outgoing, rate_column], axis=2)
            arrived = lax.all_to_all(
                outgoing, ("wall", "span"), split_axis=0, concat_axis=0, tiled=True
            )
            if substep == 0:
                fastest = jnp.max(arrived[:, :, TRACE_ROWS])
                arrived = arrived[:, :, :TRACE_ROWS]
                step_sizes = COURANT / fastest / divisors
            if fresh < slot_count:
                arrived = jnp.concatenate([arrived, received[:, fresh:]], axis=1)
            received = arrived
            lookup = jnp.concatenate(
                [table_rows, received.reshape(peers * slot_count, TRACE_ROWS)], axis=0
            )
            jump_rows = lookup.at[pointers].get(mode="promise_in_bounds") - table_rows
            lifted = jnp.einsum(
                "fvpj,fej->vpe",
                lift_big,
                jump_rows.reshape(6, local_count, TRACE_ROWS),
                precision=lax.Precision.HIGH,
            )
            combined = lifted - jnp.einsum(
                "pq,vqe->vpe", volume_block, fields, precision=lax.Precision.HIGH
            )
            change = metric_scale * jnp.einsum(
                "vw,wpe->vpe", flux_mixing, combined, precision=lax.Precision.HIGH
            )
            fields = fields + jnp.where(level_map >= lowest, step_sizes * change, 0.0)
        return (fields, cache)

    final_fields, final_cache = lax.fori_loop(0, COARSE_STEPS, coarse_step, (solution, start_cache))
    return final_fields


def solution(mesh):
    return jax.shard_map(
        body,
        mesh=mesh,
        in_specs=(
            P(None, None, ("wall", "span")),
            P(("wall", "span")),
            P(("wall", "span"), None),
            P(None, ("wall", "span")),
            P(),
            P(),
            P(),
            P(("wall", "span")),
        ),
        out_specs=P(None, None, ("wall", "span")),
        check_vma=False,
    )
```

```python
import jax
import jax.numpy as jnp
from jax import lax
from jax.sharding import PartitionSpec as P

VARIABLES = 5
DEGREE = 4
FACE_NODES = 25
TRACE_ROWS = 125
LEVELS = 4
COARSE_STEPS = 3


COURANT = 0.6


def face_traces(fields):
    local_count = fields.shape[2]
    node_cube = fields.reshape(VARIABLES, DEGREE + 1, DEGREE + 1, DEGREE + 1, local_count)
    face_list = [
        node_cube[:, 0],
        node_cube[:, -1],
        node_cube[:, :, 0],
        node_cube[:, :, -1],
        node_cube[:, :, :, 0],
        node_cube[:, :, :, -1],
    ]
    return jnp.stack(
        [face.reshape(VARIABLES, FACE_NODES, local_count) for face in face_list], axis=1
    )


def tendency(fields, nearby, volume_block, lift_block, flux_mixing, metric_scale):
    own_trace = face_traces(fields).reshape(VARIABLES, 6 * FACE_NODES, fields.shape[2])
    face_jumps = nearby - own_trace
    combined = jnp.einsum("pj,vje->vpe", lift_block, face_jumps, precision=lax.Precision.HIGH)
    combined = combined - jnp.einsum(
        "pq,vqe->vpe", volume_block, fields, precision=lax.Precision.HIGH
    )
    return metric_scale * jnp.einsum(
        "vw,wpe->vpe", flux_mixing, combined, precision=lax.Precision.HIGH
    )


def arrange(columns, local_count):
    shaped = columns.reshape(VARIABLES, FACE_NODES, 6, local_count).transpose(0, 2, 1, 3)
    return shaped.reshape(VARIABLES, 6 * FACE_NODES, local_count)


def make_table(fields):
    return face_traces(fields).transpose(0, 2, 1, 3).reshape(TRACE_ROWS, 6 * fields.shape[2])


def send_slots(outgoing):
    return lax.all_to_all(outgoing, ("wall", "span"), split_axis=1, concat_axis=1, tiled=True)


def lowest_level(substep):
    for candidate in range(LEVELS):
        if substep % 2 ** (LEVELS - 1 - candidate) == 0:
            return candidate
    return LEVELS - 1


def slot_level(slot, slot_count):
    power = 0
    while power < LEVELS - 1 and 2 ** (power + 1) * (slot_count - slot) <= slot_count:
        power = power + 1
    return max(LEVELS - 1 - power, 0)


def changed_slots(substep, slot_count):
    if substep == 0:
        return slot_count
    previous = lowest_level(substep - 1)
    levels = [slot_level(k, slot_count) for k in range(slot_count)]
    assert levels == sorted(levels, reverse=True)
    return sum(1 for level in levels if level >= previous)


def body(
    solution,
    level_map,
    send_list,
    face_partner,
    volume_block,
    lift_block,
    flux_mixing,
    metric_scale,
):
    local_count = solution.shape[2]
    peers = lax.axis_size(("wall", "span"))
    slot_count = send_list.shape[1] // peers
    send_row = send_list[0]
    pointers = face_partner.reshape(-1)
    divisors = jnp.power(2, level_map).astype(jnp.float32)
    lift_faces = lift_block.reshape(TRACE_ROWS, 6, FACE_NODES).transpose(1, 0, 2)
    lift_big = (
        jnp.eye(VARIABLES, dtype=jnp.float32)[None, :, None, :, None] * lift_faces[:, None, :, None, :]
    ).reshape(6, VARIABLES, TRACE_ROWS, TRACE_ROWS)
    substeps = 2 ** (LEVELS - 1)
    start_cache = jnp.zeros((TRACE_ROWS, peers, slot_count), jnp.float32)

    def coarse_step(coarse_index, carry):
        fields, cache = carry
        element_rates = metric_scale * (1.0 + jnp.sqrt(jnp.mean(fields * fields, axis=(0, 1))))
        local_fastest = jnp.max(element_rates)
        step_sizes = None
        received = None
        for substep in range(substeps):
            lowest = lowest_level(substep)
            fresh = changed_slots(substep, slot_count)
            trace_table = make_table(fields)
            table_rows = trace_table.T
            send_columns = send_row.reshape(peers, slot_count)[:, :fresh]
            outgoing = table_rows.at[send_columns].get(mode="promise_in_bounds")
            if substep == 0:
                rate_column = jnp.full((peers, fresh, 1), local_fastest, jnp.float32)
                outgoing = jnp.concatenate([outgoing, rate_column], axis=2)
            arrived = lax.all_to_all(
                outgoing, ("wall", "span"), split_axis=0, concat_axis=0, tiled=True
            )
            if substep == 0:
                fastest = jnp.max(arrived[:, :, TRACE_ROWS])
                arrived = arrived[:, :, :TRACE_ROWS]
                step_sizes = COURANT / fastest / divisors
            if fresh < slot_count:
                arrived = jnp.concatenate([arrived, received[:, fresh:]], axis=1)
            received = arrived
            lookup = jnp.concatenate(
                [table_rows, received.reshape(peers * slot_count, TRACE_ROWS)], axis=0
            )
            own_part = jnp.einsum(
                "fvpj,fej->vpe",
                lift_big,
                table_rows.reshape(6, local_count, TRACE_ROWS),
                precision=lax.Precision.HIGH,
            ) + jnp.einsum("pq,vqe->vpe", volume_block, fields, precision=lax.Precision.HIGH)
            near_rows = lookup.at[pointers].get(mode="promise_in_bounds")
            combined = jnp.einsum(
                "fvpj,fej->vpe",
                lift_big,
                near_rows.reshape(6, local_count, TRACE_ROWS),
                precision=lax.Precision.HIGH,
            ) - own_part
            change = metric_scale * jnp.einsum(
                "vw,wpe->vpe", flux_mixing, combined, precision=lax.Precision.HIGH
            )
            fields = fields + jnp.where(level_map >= lowest, step_sizes * change, 0.0)
        return (fields, cache)

    final_fields, final_cache = lax.fori_loop(0, COARSE_STEPS, coarse_step, (solution, start_cache))
    return final_fields


def solution(mesh):
    return jax.shard_map(
        body,
        mesh=mesh,
        in_specs=(
            P(None, None, ("wall", "span")),
            P(("wall", "span")),
            P(("wall", "span"), None),
            P(None, ("wall", "span")),
            P(),
            P(),
            P(),
            P(("wall", "span")),
        ),
        out_specs=P(None, None, ("wall", "span")),
        check_vma=False,
    )
```

```python
import jax
import jax.numpy as jnp
from jax import lax
from jax.sharding import PartitionSpec as P

VARIABLES = 5
DEGREE = 4
FACE_NODES = 25
TRACE_ROWS = 125
LEVELS = 4
COARSE_STEPS = 3


COURANT = 0.6


def face_traces(fields):
    local_count = fields.shape[2]
    node_cube = fields.reshape(VARIABLES, DEGREE + 1, DEGREE + 1, DEGREE + 1, local_count)
    face_list = [
        node_cube[:, 0],
        node_cube[:, -1],
        node_cube[:, :, 0],
        node_cube[:, :, -1],
        node_cube[:, :, :, 0],
        node_cube[:, :, :, -1],
    ]
    return jnp.stack(
        [face.reshape(VARIABLES, FACE_NODES, local_count) for face in face_list], axis=1
    )


def tendency(fields, nearby, volume_block, lift_block, flux_mixing, metric_scale):
    own_trace = face_traces(fields).reshape(VARIABLES, 6 * FACE_NODES, fields.shape[2])
    face_jumps = nearby - own_trace
    combined = jnp.einsum("pj,vje->vpe", lift_block, face_jumps, precision=lax.Precision.HIGH)
    combined = combined - jnp.einsum(
        "pq,vqe->vpe", volume_block, fields, precision=lax.Precision.HIGH
    )
    return metric_scale * jnp.einsum(
        "vw,wpe->vpe", flux_mixing, combined, precision=lax.Precision.HIGH
    )


def arrange(columns, local_count):
    shaped = columns.reshape(VARIABLES, FACE_NODES, 6, local_count).transpose(0, 2, 1, 3)
    return shaped.reshape(VARIABLES, 6 * FACE_NODES, local_count)


def make_table(fields):
    return face_traces(fields).transpose(0, 2, 1, 3).reshape(TRACE_ROWS, 6 * fields.shape[2])


def send_slots(outgoing):
    return lax.all_to_all(outgoing, ("wall", "span"), split_axis=1, concat_axis=1, tiled=True)


def lowest_level(substep):
    for candidate in range(LEVELS):
        if substep % 2 ** (LEVELS - 1 - candidate) == 0:
            return candidate
    return LEVELS - 1


def slot_level(slot, slot_count):
    power = 0
    while power < LEVELS - 1 and 2 ** (power + 1) * (slot_count - slot) <= slot_count:
        power = power + 1
    return max(LEVELS - 1 - power, 0)


def changed_slots(substep, slot_count):
    if substep == 0:
        return slot_count
    previous = lowest_level(substep - 1)
    levels = [slot_level(k, slot_count) for k in range(slot_count)]
    assert levels == sorted(levels, reverse=True)
    return sum(1 for level in levels if level >= previous)


def body(
    solution,
    level_map,
    send_list,
    face_partner,
    volume_block,
    lift_block,
    flux_mixing,
    metric_scale,
):
    local_count = solution.shape[2]
    peers = lax.axis_size(("wall", "span"))
    slot_count = send_list.shape[1] // peers
    send_row = send_list[0]
    pointers = face_partner.reshape(-1)
    divisors = jnp.power(2, level_map).astype(jnp.float32)
    lift_faces = lift_block.reshape(TRACE_ROWS, 6, FACE_NODES).transpose(1, 0, 2)
    lift_big = (
        jnp.eye(VARIABLES, dtype=jnp.float32)[None, :, None, :, None] * lift_faces[:, None, :, None, :]
    ).reshape(6, VARIABLES, TRACE_ROWS, TRACE_ROWS)
    substeps = 2 ** (LEVELS - 1)
    start_cache = jnp.zeros((TRACE_ROWS, peers, slot_count), jnp.float32)

    def coarse_step(coarse_index, carry):
        fields, cache = carry
        element_rates = metric_scale * (1.0 + jnp.sqrt(jnp.mean(fields * fields, axis=(0, 1))))
        local_fastest = jnp.max(element_rates)
        step_sizes = None
        received = None
        for substep in range(substeps):
            lowest = lowest_level(substep)
            fresh = changed_slots(substep, slot_count)
            trace_table = make_table(fields)
            table_rows = trace_table.T
            send_columns = send_row.reshape(peers, slot_count)[:, :fresh]
            outgoing = table_rows.at[send_columns].get(mode="promise_in_bounds")
            if substep == 0:
                rate_column = jnp.full((peers, fresh, 1), local_fastest, jnp.float32)
                outgoing = jnp.concatenate([outgoing, rate_column], axis=2)
            arrived = lax.all_to_all(
                outgoing, ("wall", "span"), split_axis=0, concat_axis=0, tiled=True
            )
            if substep == 0:
                fastest = jnp.max(arrived[:, :, TRACE_ROWS])
                arrived = arrived[:, :, :TRACE_ROWS]
                step_sizes = COURANT / fastest / divisors
            if fresh < slot_count:
                arrived = jnp.concatenate([arrived, received[:, fresh:]], axis=1)
            received = arrived
            lookup = jnp.concatenate(
                [table_rows, received.reshape(peers * slot_count, TRACE_ROWS)], axis=0
            )
            jump_rows = lookup.at[pointers].get(mode="promise_in_bounds") - table_rows
            lifted = jnp.einsum(
                "fvpj,fej->vpe",
                lift_big,
                jump_rows.reshape(6, local_count, TRACE_ROWS),
                precision=lax.Precision.HIGH,
            )
            combined = lifted - jnp.einsum(
                "pq,vqe->vpe", volume_block, fields, precision=lax.Precision.HIGH
            )
            mixed = sum(
                flux_mixing[:, w, None, None] * combined[None, w] for w in range(VARIABLES)
            )
            change = metric_scale * mixed
            fields = fields + jnp.where(level_map >= lowest, step_sizes * change, 0.0)
        return (fields, cache)

    final_fields, final_cache = lax.fori_loop(0, COARSE_STEPS, coarse_step, (solution, start_cache))
    return final_fields


def solution(mesh):
    return jax.shard_map(
        body,
        mesh=mesh,
        in_specs=(
            P(None, None, ("wall", "span")),
            P(("wall", "span")),
            P(("wall", "span"), None),
            P(None, ("wall", "span")),
            P(),
            P(),
            P(),
            P(("wall", "span")),
        ),
        out_specs=P(None, None, ("wall", "span")),
        check_vma=False,
    )
```

```python
import jax
import jax.numpy as jnp
from jax import lax
from jax.sharding import PartitionSpec as P

VARIABLES = 5
DEGREE = 4
FACE_NODES = 25
TRACE_ROWS = 125
LEVELS = 4
COARSE_STEPS = 3


COURANT = 0.6


def face_traces(fields):
    local_count = fields.shape[2]
    node_cube = fields.reshape(VARIABLES, DEGREE + 1, DEGREE + 1, DEGREE + 1, local_count)
    face_list = [
        node_cube[:, 0],
        node_cube[:, -1],
        node_cube[:, :, 0],
        node_cube[:, :, -1],
        node_cube[:, :, :, 0],
        node_cube[:, :, :, -1],
    ]
    return jnp.stack(
        [face.reshape(VARIABLES, FACE_NODES, local_count) for face in face_list], axis=1
    )


def tendency(fields, nearby, volume_block, lift_block, flux_mixing, metric_scale):
    own_trace = face_traces(fields).reshape(VARIABLES, 6 * FACE_NODES, fields.shape[2])
    face_jumps = nearby - own_trace
    combined = jnp.einsum("pj,vje->vpe", lift_block, face_jumps, precision=lax.Precision.HIGH)
    combined = combined - jnp.einsum(
        "pq,vqe->vpe", volume_block, fields, precision=lax.Precision.HIGH
    )
    return metric_scale * jnp.einsum(
        "vw,wpe->vpe", flux_mixing, combined, precision=lax.Precision.HIGH
    )


def arrange(columns, local_count):
    shaped = columns.reshape(VARIABLES, FACE_NODES, 6, local_count).transpose(0, 2, 1, 3)
    return shaped.reshape(VARIABLES, 6 * FACE_NODES, local_count)


def make_table(fields):
    return face_traces(fields).transpose(0, 2, 1, 3).reshape(TRACE_ROWS, 6 * fields.shape[2])


def send_slots(outgoing):
    return lax.all_to_all(outgoing, ("wall", "span"), split_axis=1, concat_axis=1, tiled=True)


def lowest_level(substep):
    for candidate in range(LEVELS):
        if substep % 2 ** (LEVELS - 1 - candidate) == 0:
            return candidate
    return LEVELS - 1


def slot_level(slot, slot_count):
    power = 0
    while power < LEVELS - 1 and 2 ** (power + 1) * (slot_count - slot) <= slot_count:
        power = power + 1
    return max(LEVELS - 1 - power, 0)


def changed_slots(substep, slot_count):
    if substep == 0:
        return slot_count
    previous = lowest_level(substep - 1)
    levels = [slot_level(k, slot_count) for k in range(slot_count)]
    assert levels == sorted(levels, reverse=True)
    return sum(1 for level in levels if level >= previous)


def body(
    solution,
    level_map,
    send_list,
    face_partner,
    volume_block,
    lift_block,
    flux_mixing,
    metric_scale,
):
    local_count = solution.shape[2]
    peers = lax.axis_size(("wall", "span"))
    slot_count = send_list.shape[1] // peers
    send_row = send_list[0]
    pointers = face_partner.reshape(-1)
    divisors = jnp.power(2, level_map).astype(jnp.float32)
    lift_faces = lift_block.reshape(TRACE_ROWS, 6, FACE_NODES).transpose(1, 0, 2)
    lift_big = (
        jnp.eye(VARIABLES, dtype=jnp.float32)[None, :, None, :, None] * lift_faces[:, None, :, None, :]
    ).reshape(6, VARIABLES, TRACE_ROWS, TRACE_ROWS)
    substeps = 2 ** (LEVELS - 1)
    start_cache = jnp.zeros((TRACE_ROWS, peers, slot_count), jnp.float32)

    def coarse_step(coarse_index, carry):
        fields, cache = carry
        element_rates = metric_scale * (1.0 + jnp.sqrt(jnp.mean(fields * fields, axis=(0, 1))))
        local_fastest = jnp.max(element_rates)
        step_sizes = None
        received = None
        for substep in range(substeps):
            lowest = lowest_level(substep)
            fresh = changed_slots(substep, slot_count)
            trace_table = make_table(fields)
            table_rows = trace_table.T
            send_columns = send_row.reshape(peers, slot_count)[:, :fresh]
            source_rows = table_rows
            if substep == 0:
                rate_row = jnp.full((1, TRACE_ROWS), local_fastest, jnp.float32)
                source_rows = jnp.concatenate([table_rows, rate_row], axis=0)
                rate_index = jnp.full((peers, 1), table_rows.shape[0], send_columns.dtype)
                send_columns = jnp.concatenate([send_columns, rate_index], axis=1)
            outgoing = source_rows.at[send_columns].get(mode="promise_in_bounds")
            arrived = lax.all_to_all(
                outgoing, ("wall", "span"), split_axis=0, concat_axis=0, tiled=True
            )
            if substep == 0:
                fastest = jnp.max(arrived[:, slot_count, 0])
                arrived = arrived[:, :slot_count]
                step_sizes = COURANT / fastest / divisors
            if fresh < slot_count:
                arrived = jnp.concatenate([arrived, received[:, fresh:]], axis=1)
            received = arrived
            lookup = jnp.concatenate(
                [table_rows, received.reshape(peers * slot_count, TRACE_ROWS)], axis=0
            )
            jump_rows = lookup.at[pointers].get(mode="promise_in_bounds") - table_rows
            lifted = jnp.einsum(
                "fvpj,fej->vpe",
                lift_big,
                jump_rows.reshape(6, local_count, TRACE_ROWS),
                precision=lax.Precision.HIGH,
            )
            combined = lifted - jnp.einsum(
                "pq,vqe->vpe", volume_block, fields, precision=lax.Precision.HIGH
            )
            change = metric_scale * jnp.einsum(
                "vw,wpe->vpe", flux_mixing, combined, precision=lax.Precision.HIGH
            )
            fields = fields + jnp.where(level_map >= lowest, step_sizes * change, 0.0)
        return (fields, cache)

    final_fields, final_cache = lax.fori_loop(0, COARSE_STEPS, coarse_step, (solution, start_cache))
    return final_fields


def solution(mesh):
    return jax.shard_map(
        body,
        mesh=mesh,
        in_specs=(
            P(None, None, ("wall", "span")),
            P(("wall", "span")),
            P(("wall", "span"), None),
            P(None, ("wall", "span")),
            P(),
            P(),
            P(),
            P(("wall", "span")),
        ),
        out_specs=P(None, None, ("wall", "span")),
        check_vma=False,
    )
```
